128 devices in a mesh: lon: 32 (over z_lo, y, x), lat: 4 (over z_hi, core).
Axes of the slice: x: 4, y: 4, z: 4 (z_hi: 2, z_lo: 2; z = z_hi * 2 + z_lo), core: 2. Of those that a mesh axis runs over, the one named last changes fastest.
Arguments:
- increment: float32 [3, 8192, 1024], P(None, 'lon', 'lat'), may hold values from -6 to 6
- depth_field: float32 [8192, 1024], P('lon', 'lat'), may hold values from 0.5 to 1.5
- coriolis: float32 [1024], P('lat'), may hold values from -0.5 to 0.5
- footprint: bfloat16 [128, 128], replicated, may hold values from -0.5 to 0.5
- channel_weights: float32 [5, 3], replicated, may hold values from -3.5 to 3.5
- track_tiles: int32 [2, 4, 32, 32], P(None, 'lat', 'lon'), may hold values from -1 to 3, as said below
- innovations: bfloat16 [2, 4, 32, 32, 5, 128, 128], P(None, 'lat', 'lon'), may hold values from -6 to 6
- obs_weights: bfloat16 [2, 4, 32, 32], P(None, 'lat', 'lon'), may hold values from 0.25 to 2
Outputs:
- gradient: float32 [3, 8192, 1024], P(None, 'lon', 'lat')
The draws below stay inside these ranges and needn't reach their ends.
Inputs may be any that keep to these rules, and one draw needn't show every extreme that they name: `track_tiles`: tiles are numbered 0 to 3 within a slab's block of a band. At every observation time, in every band, one owner observes a tile of every slab; other entries are -1 or a tile.
All inputs are finite; a program needn't handle non-finite values.
Results may differ from the reference program's by a relative error of at most 0.0028.
Values may be sent and summed in bfloat16 or wider, within the bound.
No kernel may reach another device: no remote copies, remote signals or barrier semaphores. Data moves between devices by JAX's collectives and lax.ppermute only.
A program may use at most 192 MiB of HBM per device.

```python
import math
import jax
import jax.numpy as jnp
from jax import lax

CLON = 256
CLAT = 256
TILE = 128
NCHAN = 5
STEPS = 6
OBS_TIMES = 2
SLABS = 32
BANDS = 4
NLON = 8192
NLAT = 1024
TILES_DEV = 4


def draw_track_tiles(key, part):
    key_tiles = jax.random.fold_in(key, 11)
    key_keep = jax.random.fold_in(key, 12)
    key_busy = jax.random.fold_in(key, 13)
    shape = (OBS_TIMES, BANDS, SLABS, SLABS)
    tiles = jax.random.randint(key_tiles, shape, 0, TILES_DEV)
    keep = jax.random.randint(key_keep, shape, 0, 5) < 2
    busy = jax.random.randint(key_busy, (OBS_TIMES, BANDS, 1, 1), 0, SLABS)
    owners = jnp.arange(SLABS, dtype=jnp.int32)[None, None, None, :]
    sources = jnp.arange(SLABS, dtype=jnp.int32)[None, None, :, None]
    is_busy = owners == busy
    keep = keep | is_busy
    tiles = jnp.where(is_busy & (sources == 0), TILES_DEV - 1, tiles)
    empty_spot = (owners == (busy + 1) % SLABS) & (sources == 0)
    keep = keep & jnp.logical_not(empty_spot)
    return jnp.where(keep, tiles, -1).astype(jnp.int32)


def block_levels(rng, extent, cuts, least, high):
    loudness = 1.0
    for dim, shards_of in cuts:
        draws = jax.random.uniform(jax.random.fold_in(jax.random.fold_in(rng, 6), dim), (shards_of,), jnp.float32, least / len(cuts), high / len(cuts))
        loudness = loudness * jnp.repeat(jnp.exp(draws), extent[dim] // shards_of).reshape((-1,) + (1,) * (len(extent) - 1 - dim))
    return loudness


def scatter_about(key, dims, scale, reach, split=(), kind=jnp.bfloat16):
    drawn = jax.random.normal(key, dims, jnp.float32) * scale
    if len(split) > 0:
        drawn = block_levels(key, dims, split, -0.22, 0.18) * drawn
    return jnp.clip(drawn, min=-reach, max=reach).astype(kind)


def setup_inputs(seed: int = 0) -> dict:
    keys = jax.random.split(jax.random.key(seed), 9)
    increment = scatter_about(keys[0], (3, NLON, NLAT), 1.0, 6.0, ((1, 32), (2, 4)), jnp.float32)
    depth_field = jnp.clip(jnp.exp(math.log(1.5) - 1.0986123 * jax.random.uniform(keys[1], (NLON, NLAT), jnp.float32) ** block_levels(keys[1], (NLON, NLAT), ((0, 32), (1, 4)), -0.2, 0.2)), 0.5, 1.5)
    coriolis = jnp.clip(jax.random.uniform(keys[2], (NLAT,), jnp.float32, -0.5, 0.5) * block_levels(keys[2], (NLAT,), ((0, 4),), -0.4, 0.0), -0.5, 0.5)
    footprint = scatter_about(keys[3], (TILE, TILE), TILE ** -0.5, 0.5)
    channel_weights = scatter_about(keys[4], (NCHAN, 3), 3 ** -0.5, 3.5, (), jnp.float32)
    track_tiles = draw_track_tiles(jax.random.fold_in(keys[8], 71), 0)
    innovations = scatter_about(keys[6], (OBS_TIMES, BANDS, SLABS, SLABS, NCHAN, TILE, TILE), 1.0, 6.0, ((1, 4), (2, 32)))
    obs_weights = jnp.clip(jnp.exp(math.log(2.0) - 2.0794415 * jax.random.uniform(keys[7], (OBS_TIMES, BANDS, SLABS, SLABS), jnp.float32) ** block_levels(keys[7], (OBS_TIMES, BANDS, SLABS, SLABS), ((1, 4), (2, 32)), -0.2, 0.2)), 0.25, 2.0).astype(jnp.bfloat16)
    return {"increment": increment, "depth_field": depth_field, "coriolis": coriolis, "footprint": footprint, "channel_weights": channel_weights, "track_tiles": track_tiles, "innovations": innovations, "obs_weights": obs_weights}


COURANT = 0.7


def lon_diff(values):
    return 0.5 * (jnp.roll(values, -1, axis=0) - jnp.roll(values, 1, axis=0))


def lat_diff(values):
    padded = jnp.pad(values, ((0, 0), (1, 1)))
    return 0.5 * (padded[:, 2:] - padded[:, :-2])


def tangent_step(east_wind, north_wind, height, depth_field, coriolis):
    height_next = height - COURANT * (lon_diff(depth_field * east_wind) + lat_diff(depth_field * north_wind))
    east_next = east_wind + coriolis * north_wind - COURANT * lon_diff(height_next)
    north_next = north_wind - coriolis * east_next - COURANT * lat_diff(height_next)
    return east_next, north_next, height_next


def adjoint_step(east_adj, north_adj, height_adj, depth_field, coriolis):
    east_once = east_adj - coriolis * north_adj
    height_once = height_adj + COURANT * (lat_diff(north_adj) + lon_diff(east_once))
    east_prev = east_once + COURANT * depth_field * lon_diff(height_once)
    north_prev = north_adj + coriolis * east_once + COURANT * depth_field * lat_diff(height_once)
    return east_prev, north_prev, height_once


def to_tiles(fields):
    blocks = fields.reshape(3, SLABS, CLON // TILE, TILE, BANDS, CLAT // TILE, TILE)
    blocks = blocks.transpose(4, 1, 2, 5, 0, 3, 6)
    return blocks.reshape(BANDS, SLABS, TILES_DEV, 3, TILE, TILE)


def from_tiles(pieces):
    blocks = pieces.reshape(BANDS, SLABS, CLON // TILE, CLAT // TILE, 3, TILE, TILE)
    blocks = blocks.transpose(4, 1, 2, 5, 0, 3, 6)
    return blocks.reshape(3, NLON, NLAT)


def residual_adjoint(arrived, innov, weights, footprint, channel_weights):
    highest = lax.Precision.HIGHEST
    foot_wide = footprint.astype(jnp.float32)
    spread = jnp.einsum("kcab,bd->kcad", arrived.astype(jnp.float32), foot_wide, precision=highest)
    radiance = jnp.einsum("hc,kcad->khad", channel_weights, spread, precision=highest)
    weighted = weights.astype(jnp.float32)[:, None, None, None] * (radiance - innov.astype(jnp.float32))
    back = jnp.einsum("hc,khad->kcad", channel_weights, weighted, precision=highest).astype(jnp.bfloat16)
    return jnp.einsum("kcad,bd->kcab", back.astype(jnp.float32), foot_wide, precision=highest)


def observe(state, tracks_now, innov_now, weights_now, footprint, channel_weights):
    tiles = to_tiles(jnp.stack(state)).astype(jnp.bfloat16)

    def per_owner(operands):
        incoming, innov, weights = operands
        return residual_adjoint(incoming, innov, weights, footprint, channel_weights)

    def per_band(operands):
        tiles_band, track_band, innov_band, weight_band = operands
        is_valid = track_band >= 0
        tile_index = jnp.maximum(track_band, 0).astype(jnp.int32)
        sources = jnp.arange(SLABS, dtype=jnp.int32)
        outgoing = tiles_band[sources[:, None], tile_index]
        incoming = jnp.swapaxes(outgoing, 0, 1)
        answer = lax.map(per_owner, (incoming, innov_band, weight_band))
        returned = jnp.swapaxes(answer, 0, 1)
        numbers = jnp.arange(TILES_DEV, dtype=jnp.int32)
        one_hot = ((tile_index[:, :, None] == numbers[None, None, :]) & is_valid[:, :, None]).astype(jnp.float32)
        return jnp.einsum("sot,socab->stcab", one_hot, returned, precision=lax.Precision.HIGHEST)

    forcing = lax.map(per_band, (tiles, tracks_now, innov_now, weights_now))
    return from_tiles(forcing)


def reference(increment, depth_field, coriolis, footprint, channel_weights, track_tiles, innovations, obs_weights):
    interval = STEPS // OBS_TIMES
    east_wind, north_wind, height = increment[0], increment[1], increment[2]
    forcings = []
    for step_index in range(STEPS):
        east_wind, north_wind, height = tangent_step(east_wind, north_wind, height, depth_field, coriolis)
        if (step_index + 1) % interval == 0:
            obs_index = (step_index + 1) // interval - 1
            forcings.append(observe((east_wind, north_wind, height), track_tiles[obs_index], innovations[obs_index], obs_weights[obs_index], footprint, channel_weights))
    east_adj = jnp.zeros_like(east_wind)
    north_adj = jnp.zeros_like(east_wind)
    height_adj = jnp.zeros_like(east_wind)
    for step_index in range(STEPS, 0, -1):
        if step_index % interval == 0:
            forcing = forcings[step_index // interval - 1]
            east_adj = east_adj + forcing[0]
            north_adj = north_adj + forcing[1]
            height_adj = height_adj + forcing[2]
        east_adj, north_adj, height_adj = adjoint_step(east_adj, north_adj, height_adj, depth_field, coriolis)
    return increment + jnp.stack([east_adj, north_adj, height_adj])
```

```python
import jax
import jax.numpy as jnp
from jax import lax
from jax.sharding import PartitionSpec as P

TILE = 128
STEPS = 6
OBS_TIMES = 2
HALO = 2 * STEPS


COURANT = 0.7


def extend_lon(x, width):
    peers, length = lax.axis_size("lon"), x.shape[-2]
    up = [(i, (i + 1) % peers) for i in range(peers)]
    down = [(j, i) for i, j in up]
    before = lax.ppermute(x[..., length - width :, :], "lon", up)
    after = lax.ppermute(x[..., :width, :], "lon", down)
    return jnp.concatenate([before, x, after], axis=-2)


def extend_lat(x, width):
    peers, length = lax.axis_size("lat"), x.shape[-1]
    up = [(i, i + 1) for i in range(peers - 1)]
    down = [(j, i) for i, j in up]
    before = lax.ppermute(x[..., length - width :], "lat", up)
    after = lax.ppermute(x[..., :width], "lat", down)
    return jnp.concatenate([before, x, after], axis=-1)


def extend(x, width):
    return extend_lat(extend_lon(x, width), width)


def lon_diff(values):
    return 0.5 * (jnp.roll(values, -1, axis=0) - jnp.roll(values, 1, axis=0))


def lat_diff(values):
    return 0.5 * (jnp.roll(values, -1, axis=1) - jnp.roll(values, 1, axis=1))


def tangent_step(east_wind, north_wind, height, depth_field, coriolis, inside):
    height_next = height - COURANT * (
        lon_diff(depth_field * east_wind) + lat_diff(depth_field * north_wind)
    )
    height_next = jnp.where(inside, height_next, 0.0)
    east_next = east_wind + coriolis * north_wind - COURANT * lon_diff(height_next)
    north_next = north_wind - coriolis * east_next - COURANT * lat_diff(height_next)
    north_next = jnp.where(inside, north_next, 0.0)
    return (east_next, north_next, height_next)


def adjoint_step(east_adj, north_adj, height_adj, depth_field, coriolis, inside):
    east_once = east_adj - coriolis * north_adj
    height_once = height_adj + COURANT * (lat_diff(north_adj) + lon_diff(east_once))
    height_once = jnp.where(inside, height_once, 0.0)
    east_prev = east_once + COURANT * depth_field * lon_diff(height_once)
    north_prev = north_adj + coriolis * east_once + COURANT * depth_field * lat_diff(height_once)
    north_prev = jnp.where(inside, north_prev, 0.0)
    return (east_prev, north_prev, height_once)


def to_tiles(block_data):
    fields, row_total, col_total = block_data.shape
    blocks = block_data.reshape(fields, row_total // TILE, TILE, col_total // TILE, TILE)
    return blocks.transpose(1, 3, 0, 2, 4).reshape(-1, fields, TILE, TILE)


def from_tiles(pieces, row_total, col_total):
    fields = pieces.shape[1]
    blocks = pieces.reshape(row_total // TILE, col_total // TILE, fields, TILE, TILE)
    return blocks.transpose(2, 0, 3, 1, 4).reshape(fields, row_total, col_total)


def observe(state, track_row, innov_row, weight_row, footprint, channel_weights):
    highest = lax.Precision.HIGHEST
    tiles = to_tiles(state).astype(jnp.bfloat16)
    spread = jnp.einsum("jcab,bd->jcad", tiles, footprint, preferred_element_type=jnp.float32)
    radiance = jnp.einsum("hc,jcad->jhad", channel_weights, spread, precision=highest)
    is_valid = track_row >= 0
    tile_index = jnp.maximum(track_row, 0)
    chosen = jnp.take(radiance, tile_index, axis=0)
    weighted = weight_row.astype(jnp.float32)[:, None, None, None] * (
        chosen - innov_row.astype(jnp.float32)
    )
    back = jnp.einsum("hc,ohad->ocad", channel_weights, weighted, precision=highest).astype(
        jnp.bfloat16
    )
    numbers = jnp.arange(tiles.shape[0], dtype=jnp.int32)
    one_hot = ((tile_index[:, None] == numbers[None, :]) & is_valid[:, None]).astype(jnp.float32)
    summed = jnp.einsum("ot,ocad->tcad", one_hot, back.astype(jnp.float32), precision=highest)
    forcing = jnp.einsum(
        "tcad,bd->tcab", summed, footprint.astype(jnp.float32), precision=highest
    )
    return from_tiles(forcing, state.shape[1], state.shape[2])


def on_device(
    increment,
    depth_field,
    coriolis,
    footprint,
    channel_weights,
    track_tiles,
    innovations,
    obs_weights,
):
    interval = STEPS // OBS_TIMES
    rows, cols = depth_field.shape
    band = lax.axis_index("lat")
    lat_total = cols * lax.axis_size("lat")

    innov = innovations[:, 0, 0]
    innov = lax.all_to_all(innov, "lon", split_axis=1, concat_axis=1, tiled=True)
    weights = obs_weights[:, 0, 0]
    weights = lax.all_to_all(weights, "lon", split_axis=1, concat_axis=1, tiled=True)
    tracks = track_tiles[:, 0, 0]

    lat_global = band * cols - HALO + jnp.arange(cols + 2 * HALO, dtype=jnp.int32)
    inside = ((lat_global >= 0) & (lat_global < lat_total))[None, :]
    cor = extend_lat(coriolis[None, :], HALO)

    fields = extend(jnp.concatenate([increment, depth_field[None]], axis=0), HALO)
    east_wind, north_wind, height, depth = fields[0], fields[1], fields[2], fields[3]
    inner = (slice(HALO, HALO + rows), slice(HALO, HALO + cols))

    forcings = []
    for step_index in range(STEPS):
        east_wind, north_wind, height = tangent_step(
            east_wind, north_wind, height, depth, cor, inside
        )
        if (step_index + 1) % interval == 0:
            obs_index = (step_index + 1) // interval - 1
            state = jnp.stack([east_wind[inner], north_wind[inner], height[inner]])
            forcing = observe(
                state,
                tracks[obs_index],
                innov[obs_index],
                weights[obs_index],
                footprint,
                channel_weights,
            )
            forcings.append(extend(forcing, HALO))

    east_adj = jnp.zeros_like(depth)
    north_adj = jnp.zeros_like(depth)
    height_adj = jnp.zeros_like(depth)
    for step_index in range(STEPS, 0, -1):
        if step_index % interval == 0:
            forcing = forcings[step_index // interval - 1]
            east_adj = east_adj + forcing[0]
            north_adj = north_adj + forcing[1]
            height_adj = height_adj + forcing[2]
        east_adj, north_adj, height_adj = adjoint_step(
            east_adj, north_adj, height_adj, depth, cor, inside
        )
    adjoint = jnp.stack([east_adj[inner], north_adj[inner], height_adj[inner]])
    return increment + adjoint


def solution(mesh):
    return jax.shard_map(
        on_device,
        mesh=mesh,
        in_specs=(
            P(None, "lon", "lat"),
            P("lon", "lat"),
            P("lat"),
            P(),
            P(),
            P(None, "lat", "lon", None),
            P(None, "lat", "lon", None, None, None, None),
            P(None, "lat", "lon", None),
        ),
        out_specs=P(None, "lon", "lat"),
        check_vma=False,
    )
```

```python
import jax
import jax.numpy as jnp
from jax import lax
from jax.sharding import PartitionSpec as P

TILE = 128
STEPS = 6
OBS_TIMES = 2
HALO = 2 * STEPS


COURANT = 0.7


def extend_lon(x, width):
    peers, length = lax.axis_size("lon"), x.shape[-2]
    up = [(i, (i + 1) % peers) for i in range(peers)]
    down = [(j, i) for i, j in up]
    before = lax.ppermute(x[..., length - width :, :], "lon", up)
    after = lax.ppermute(x[..., :width, :], "lon", down)
    return jnp.concatenate([before, x, after], axis=-2)


def extend_lat(x, width):
    peers, length = lax.axis_size("lat"), x.shape[-1]
    up = [(i, i + 1) for i in range(peers - 1)]
    down = [(j, i) for i, j in up]
    before = lax.ppermute(x[..., length - width :], "lat", up)
    after = lax.ppermute(x[..., :width], "lat", down)
    return jnp.concatenate([before, x, after], axis=-1)


def extend(x, width):
    return extend_lat(extend_lon(x, width), width)


def lon_diff(values):
    return 0.5 * (jnp.roll(values, -1, axis=0) - jnp.roll(values, 1, axis=0))


def lat_diff(values):
    return 0.5 * (jnp.roll(values, -1, axis=1) - jnp.roll(values, 1, axis=1))


def tangent_step(east_wind, north_wind, height, depth_field, coriolis, inside):
    height_next = height - COURANT * (
        lon_diff(depth_field * east_wind) + lat_diff(depth_field * north_wind)
    )
    height_next = jnp.where(inside, height_next, 0.0)
    east_next = east_wind + coriolis * north_wind - COURANT * lon_diff(height_next)
    north_next = north_wind - coriolis * east_next - COURANT * lat_diff(height_next)
    north_next = jnp.where(inside, north_next, 0.0)
    return (east_next, north_next, height_next)


def adjoint_step(east_adj, north_adj, height_adj, depth_field, coriolis, inside):
    east_once = east_adj - coriolis * north_adj
    height_once = height_adj + COURANT * (lat_diff(north_adj) + lon_diff(east_once))
    height_once = jnp.where(inside, height_once, 0.0)
    east_prev = east_once + COURANT * depth_field * lon_diff(height_once)
    north_prev = north_adj + coriolis * east_once + COURANT * depth_field * lat_diff(height_once)
    north_prev = jnp.where(inside, north_prev, 0.0)
    return (east_prev, north_prev, height_once)


def to_tiles(block_data):
    fields, row_total, col_total = block_data.shape
    blocks = block_data.reshape(fields, row_total // TILE, TILE, col_total // TILE, TILE)
    return blocks.transpose(1, 3, 0, 2, 4).reshape(-1, fields, TILE, TILE)


def from_tiles(pieces, row_total, col_total):
    fields = pieces.shape[1]
    blocks = pieces.reshape(row_total // TILE, col_total // TILE, fields, TILE, TILE)
    return blocks.transpose(2, 0, 3, 1, 4).reshape(fields, row_total, col_total)


def observe(state, track_row, innov_row, weight_row, footprint, channel_weights):
    tiles = to_tiles(state).astype(jnp.bfloat16)
    count, fields = tiles.shape[0], tiles.shape[1]
    channels = channel_weights.shape[0]
    spread = jnp.einsum("jcab,bd->jcad", tiles, footprint, preferred_element_type=jnp.float32)
    is_valid = track_row >= 0
    tile_index = jnp.maximum(track_row, 0)
    index = tile_index[:, None, None]
    scale = weight_row.astype(jnp.float32)[:, None, None]
    weighted = []
    for h in range(channels):
        radiance = channel_weights[h, 0] * spread[:, 0]
        for c in range(1, fields):
            radiance = radiance + channel_weights[h, c] * spread[:, c]
        chosen = radiance[count - 1]
        for j in range(count - 2, -1, -1):
            chosen = jnp.where(index == j, radiance[j], chosen)
        weighted.append(scale * (chosen - innov_row[:, h].astype(jnp.float32)))
    back = []
    for c in range(fields):
        mixed = channel_weights[0, c] * weighted[0]
        for h in range(1, channels):
            mixed = mixed + channel_weights[h, c] * weighted[h]
        back.append(mixed.astype(jnp.bfloat16).astype(jnp.float32))
    back = jnp.stack(back, axis=1)
    summed = []
    for j in range(count):
        keep = (is_valid & (tile_index == j))[:, None, None, None]
        summed.append(jnp.sum(jnp.where(keep, back, 0.0), axis=0))
    summed = jnp.stack(summed)
    forcing = jnp.einsum(
        "tcad,bd->tcab", summed, footprint.astype(jnp.float32), precision=lax.Precision.HIGHEST
    )
    return from_tiles(forcing, state.shape[1], state.shape[2])


def on_device(
    increment,
    depth_field,
    coriolis,
    footprint,
    channel_weights,
    track_tiles,
    innovations,
    obs_weights,
):
    interval = STEPS // OBS_TIMES
    rows, cols = depth_field.shape
    band = lax.axis_index("lat")
    lat_total = cols * lax.axis_size("lat")

    innov = [
        lax.all_to_all(innovations[t, 0, 0], "lon", split_axis=0, concat_axis=0, tiled=True)
        for t in range(OBS_TIMES)
    ]
    weights = obs_weights[:, 0, 0]
    weights = lax.all_to_all(weights, "lon", split_axis=1, concat_axis=1, tiled=True)
    tracks = track_tiles[:, 0, 0]

    lat_global = band * cols - HALO + jnp.arange(cols + 2 * HALO, dtype=jnp.int32)
    inside = ((lat_global >= 0) & (lat_global < lat_total))[None, :]
    cor = extend_lat(coriolis[None, :], HALO)

    fields = extend(jnp.concatenate([increment, depth_field[None]], axis=0), HALO)
    east_wind, north_wind, height, depth = fields[0], fields[1], fields[2], fields[3]
    inner = (slice(HALO, HALO + rows), slice(HALO, HALO + cols))

    forcings = []
    for step_index in range(STEPS):
        east_wind, north_wind, height = tangent_step(
            east_wind, north_wind, height, depth, cor, inside
        )
        if (step_index + 1) % interval == 0:
            obs_index = (step_index + 1) // interval - 1
            state = jnp.stack([east_wind[inner], north_wind[inner], height[inner]])
            forcing = observe(
                state,
                tracks[obs_index],
                innov[obs_index],
                weights[obs_index],
                footprint,
                channel_weights,
            )
            forcings.append(extend(forcing, HALO))

    east_adj = jnp.zeros_like(depth)
    north_adj = jnp.zeros_like(depth)
    height_adj = jnp.zeros_like(depth)
    for step_index in range(STEPS, 0, -1):
        if step_index % interval == 0:
            forcing = forcings[step_index // interval - 1]
            east_adj = east_adj + forcing[0]
            north_adj = north_adj + forcing[1]
            height_adj = height_adj + forcing[2]
        east_adj, north_adj, height_adj = adjoint_step(
            east_adj, north_adj, height_adj, depth, cor, inside
        )
    adjoint = jnp.stack([east_adj[inner], north_adj[inner], height_adj[inner]])
    return increment + adjoint


def solution(mesh):
    return jax.shard_map(
        on_device,
        mesh=mesh,
        in_specs=(
            P(None, "lon", "lat"),
            P("lon", "lat"),
            P("lat"),
            P(),
            P(),
            P(None, "lat", "lon", None),
            P(None, "lat", "lon", None, None, None, None),
            P(None, "lat", "lon", None),
        ),
        out_specs=P(None, "lon", "lat"),
        check_vma=False,
    )
```

```python
import jax
import jax.numpy as jnp
from jax import lax
from jax.sharding import PartitionSpec as P
from jax.experimental import pallas as pl
from jax.experimental.pallas import tpu as pltpu

TILE = 128
STEPS = 6
OBS_TIMES = 2
HALO = 2 * STEPS
OWNERS_STEP = 4


COURANT = 0.7


def extend_lon(x, width):
    peers, length = lax.axis_size("lon"), x.shape[-2]
    up = [(i, (i + 1) % peers) for i in range(peers)]
    down = [(j, i) for i, j in up]
    before = lax.ppermute(x[..., length - width :, :], "lon", up)
    after = lax.ppermute(x[..., :width, :], "lon", down)
    return jnp.concatenate([before, x, after], axis=-2)


def extend_lat(x, width):
    peers, length = lax.axis_size("lat"), x.shape[-1]
    up = [(i, i + 1) for i in range(peers - 1)]
    down = [(j, i) for i, j in up]
    before = lax.ppermute(x[..., length - width :], "lat", up)
    after = lax.ppermute(x[..., :width], "lat", down)
    return jnp.concatenate([before, x, after], axis=-1)


def extend(x, width):
    return extend_lat(extend_lon(x, width), width)


def lon_diff(values):
    return 0.5 * (jnp.roll(values, -1, axis=0) - jnp.roll(values, 1, axis=0))


def lat_diff(values):
    return 0.5 * (jnp.roll(values, -1, axis=1) - jnp.roll(values, 1, axis=1))


def tangent_step(east_wind, north_wind, height, depth_field, coriolis, inside):
    height_next = height - COURANT * (
        lon_diff(depth_field * east_wind) + lat_diff(depth_field * north_wind)
    )
    height_next = jnp.where(inside, height_next, 0.0)
    east_next = east_wind + coriolis * north_wind - COURANT * lon_diff(height_next)
    north_next = north_wind - coriolis * east_next - COURANT * lat_diff(height_next)
    north_next = jnp.where(inside, north_next, 0.0)
    return (east_next, north_next, height_next)


def adjoint_step(east_adj, north_adj, height_adj, depth_field, coriolis, inside):
    east_once = east_adj - coriolis * north_adj
    height_once = height_adj + COURANT * (lat_diff(north_adj) + lon_diff(east_once))
    height_once = jnp.where(inside, height_once, 0.0)
    east_prev = east_once + COURANT * depth_field * lon_diff(height_once)
    north_prev = north_adj + coriolis * east_once + COURANT * depth_field * lat_diff(height_once)
    north_prev = jnp.where(inside, north_prev, 0.0)
    return (east_prev, north_prev, height_once)


def to_tiles(block_data):
    fields, row_total, col_total = block_data.shape
    blocks = block_data.reshape(fields, row_total // TILE, TILE, col_total // TILE, TILE)
    return blocks.transpose(1, 3, 0, 2, 4).reshape(-1, fields, TILE, TILE)


def from_tiles(pieces, row_total, col_total):
    fields = pieces.shape[1]
    blocks = pieces.reshape(row_total // TILE, col_total // TILE, fields, TILE, TILE)
    return blocks.transpose(2, 0, 3, 1, 4).reshape(fields, row_total, col_total)


def residual_kernel(index_ref, valid_ref, scale_ref, weight_ref, spread_ref, innov_ref, out_ref, radiance_ref):
    step = pl.program_id(0)
    tiles, fields = spread_ref.shape[0], spread_ref.shape[1]
    channels = radiance_ref.shape[1]

    @pl.when(step == 0)
    def _():
        for j in range(tiles):
            for h in range(channels):
                acc = weight_ref[h * fields] * spread_ref[j, 0]
                for c in range(1, fields):
                    acc = acc + weight_ref[h * fields + c] * spread_ref[j, c]
                radiance_ref[j, h] = acc
        out_ref[...] = jnp.zeros_like(out_ref)

    for k in range(OWNERS_STEP):
        owner = step * OWNERS_STEP + k
        j = index_ref[owner]
        scale = scale_ref[owner]

        @pl.when(valid_ref[owner] != 0)
        def _():
            weighted = [
                scale * (radiance_ref[j, h] - innov_ref[k, h].astype(jnp.float32))
                for h in range(channels)
            ]
            for c in range(fields):
                mixed = weight_ref[c] * weighted[0]
                for h in range(1, channels):
                    mixed = mixed + weight_ref[h * fields + c] * weighted[h]
                out_ref[j, c] = out_ref[j, c] + mixed.astype(jnp.bfloat16).astype(jnp.float32)


def residual_sums(spread, innov, index, valid, scale, channel_weights):
    tiles, fields = spread.shape[0], spread.shape[1]
    owners, channels = innov.shape[0], innov.shape[1]
    smem = pl.BlockSpec(memory_space=pltpu.SMEM)
    return pl.pallas_call(
        residual_kernel,
        grid=(owners // OWNERS_STEP,),
        in_specs=[
            smem,
            smem,
            smem,
            smem,
            pl.BlockSpec(spread.shape, lambda s: (0, 0, 0, 0)),
            pl.BlockSpec((OWNERS_STEP,) + innov.shape[1:], lambda s: (s, 0, 0, 0)),
        ],
        out_specs=pl.BlockSpec(spread.shape, lambda s: (0, 0, 0, 0)),
        out_shape=jax.ShapeDtypeStruct(spread.shape, jnp.float32),
        scratch_shapes=[pltpu.VMEM((tiles, channels) + spread.shape[2:], jnp.float32)],
        compiler_params=pltpu.CompilerParams(dimension_semantics=("arbitrary",)),
    )(index, valid, scale, channel_weights.reshape(-1), spread, innov)


def observe(state, track_row, innov_row, weight_row, footprint, channel_weights):
    tiles = to_tiles(state).astype(jnp.bfloat16)
    spread = jnp.einsum("jcab,bd->jcad", tiles, footprint, preferred_element_type=jnp.float32)
    index = jnp.clip(track_row, 0, tiles.shape[0] - 1).astype(jnp.int32)
    valid = (track_row >= 0).astype(jnp.int32)
    scale = weight_row.astype(jnp.float32)
    summed = residual_sums(spread, innov_row, index, valid, scale, channel_weights)
    forcing = jnp.einsum(
        "tcad,bd->tcab", summed, footprint.astype(jnp.float32), precision=lax.Precision.HIGHEST
    )
    return from_tiles(forcing, state.shape[1], state.shape[2])


def on_device(
    increment,
    depth_field,
    coriolis,
    footprint,
    channel_weights,
    track_tiles,
    innovations,
    obs_weights,
):
    interval = STEPS // OBS_TIMES
    rows, cols = depth_field.shape
    band = lax.axis_index("lat")
    lat_total = cols * lax.axis_size("lat")

    innov = [
        lax.all_to_all(innovations[t, 0, 0], "lon", split_axis=0, concat_axis=0, tiled=True)
        for t in range(OBS_TIMES)
    ]
    weights = obs_weights[:, 0, 0]
    weights = lax.all_to_all(weights, "lon", split_axis=1, concat_axis=1, tiled=True)
    tracks = track_tiles[:, 0, 0]

    lat_global = band * cols - HALO + jnp.arange(cols + 2 * HALO, dtype=jnp.int32)
    inside = ((lat_global >= 0) & (lat_global < lat_total))[None, :]
    cor = extend_lat(coriolis[None, :], HALO)

    fields = extend(jnp.concatenate([increment, depth_field[None]], axis=0), HALO)
    east_wind, north_wind, height, depth = fields[0], fields[1], fields[2], fields[3]
    inner = (slice(HALO, HALO + rows), slice(HALO, HALO + cols))

    forcings = []
    for step_index in range(STEPS):
        east_wind, north_wind, height = tangent_step(
            east_wind, north_wind, height, depth, cor, inside
        )
        if (step_index + 1) % interval == 0:
            obs_index = (step_index + 1) // interval - 1
            state = jnp.stack([east_wind[inner], north_wind[inner], height[inner]])
            forcing = observe(
                state,
                tracks[obs_index],
                innov[obs_index],
                weights[obs_index],
                footprint,
                channel_weights,
            )
            forcings.append(extend(forcing, HALO))

    east_adj = jnp.zeros_like(depth)
    north_adj = jnp.zeros_like(depth)
    height_adj = jnp.zeros_like(depth)
    for step_index in range(STEPS, 0, -1):
        if step_index % interval == 0:
            forcing = forcings[step_index // interval - 1]
            east_adj = east_adj + forcing[0]
            north_adj = north_adj + forcing[1]
            height_adj = height_adj + forcing[2]
        east_adj, north_adj, height_adj = adjoint_step(
            east_adj, north_adj, height_adj, depth, cor, inside
        )
    adjoint = jnp.stack([east_adj[inner], north_adj[inner], height_adj[inner]])
    return increment + adjoint


def solution(mesh):
    return jax.shard_map(
        on_device,
        mesh=mesh,
        in_specs=(
            P(None, "lon", "lat"),
            P("lon", "lat"),
            P("lat"),
            P(),
            P(),
            P(None, "lat", "lon", None),
            P(None, "lat", "lon", None, None, None, None),
            P(None, "lat", "lon", None),
        ),
        out_specs=P(None, "lon", "lat"),
        check_vma=False,
    )
```

```python
import jax
import jax.numpy as jnp
from jax import lax
from jax.sharding import PartitionSpec as P
from jax.experimental import pallas as pl
from jax.experimental.pallas import tpu as pltpu

TILE = 128
STEPS = 6
OBS_TIMES = 2
HALO = 2 * STEPS
OWNERS_STEP = 4


COURANT = 0.7


def extend_lon(x, width):
    peers, length = lax.axis_size("lon"), x.shape[-2]
    up = [(i, (i + 1) % peers) for i in range(peers)]
    down = [(j, i) for i, j in up]
    before = lax.ppermute(x[..., length - width :, :], "lon", up)
    after = lax.ppermute(x[..., :width, :], "lon", down)
    return jnp.concatenate([before, x, after], axis=-2)


def extend_lat(x, width):
    peers, length = lax.axis_size("lat"), x.shape[-1]
    up = [(i, i + 1) for i in range(peers - 1)]
    down = [(j, i) for i, j in up]
    before = lax.ppermute(x[..., length - width :], "lat", up)
    after = lax.ppermute(x[..., :width], "lat", down)
    return jnp.concatenate([before, x, after], axis=-1)


def extend(x, width):
    return extend_lat(extend_lon(x, width), width)


def lon_diff(values):
    return 0.5 * (jnp.roll(values, -1, axis=0) - jnp.roll(values, 1, axis=0))


def lat_diff(values):
    return 0.5 * (jnp.roll(values, -1, axis=1) - jnp.roll(values, 1, axis=1))


def tangent_step(east_wind, north_wind, height, depth_field, coriolis, inside):
    height_next = height - COURANT * (
        lon_diff(depth_field * east_wind) + lat_diff(depth_field * north_wind)
    )
    height_next = jnp.where(inside, height_next, 0.0)
    east_next = east_wind + coriolis * north_wind - COURANT * lon_diff(height_next)
    north_next = north_wind - coriolis * east_next - COURANT * lat_diff(height_next)
    north_next = jnp.where(inside, north_next, 0.0)
    return (east_next, north_next, height_next)


def adjoint_step(east_adj, north_adj, height_adj, depth_field, coriolis, inside):
    east_once = east_adj - coriolis * north_adj
    height_once = height_adj + COURANT * (lat_diff(north_adj) + lon_diff(east_once))
    height_once = jnp.where(inside, height_once, 0.0)
    east_prev = east_once + COURANT * depth_field * lon_diff(height_once)
    north_prev = north_adj + coriolis * east_once + COURANT * depth_field * lat_diff(height_once)
    north_prev = jnp.where(inside, north_prev, 0.0)
    return (east_prev, north_prev, height_once)


def to_tiles(block_data):
    fields, row_total, col_total = block_data.shape
    blocks = block_data.reshape(fields, row_total // TILE, TILE, col_total // TILE, TILE)
    return blocks.transpose(1, 3, 0, 2, 4).reshape(-1, fields, TILE, TILE)


def from_tiles(pieces, row_total, col_total):
    fields = pieces.shape[1]
    blocks = pieces.reshape(row_total // TILE, col_total // TILE, fields, TILE, TILE)
    return blocks.transpose(2, 0, 3, 1, 4).reshape(fields, row_total, col_total)


def residual_kernel(index_ref, valid_ref, scale_ref, weight_ref, spread_ref, innov_ref, out_ref, radiance_ref):
    step = pl.program_id(0)
    tiles, fields = spread_ref.shape[0], spread_ref.shape[1]
    channels = radiance_ref.shape[1]

    @pl.when(step == 0)
    def _():
        for j in range(tiles):
            for h in range(channels):
                acc = weight_ref[h * fields] * spread_ref[j, 0]
                for c in range(1, fields):
                    acc = acc + weight_ref[h * fields + c] * spread_ref[j, c]
                radiance_ref[j, h] = acc
        out_ref[...] = jnp.zeros_like(out_ref)

    for k in range(OWNERS_STEP):
        owner = step * OWNERS_STEP + k
        j = index_ref[owner]
        scale = scale_ref[owner]

        @pl.when(valid_ref[owner] != 0)
        def _():
            weighted = [
                scale * (radiance_ref[j, h] - innov_ref[k, h].astype(jnp.float32))
                for h in range(channels)
            ]
            for c in range(fields):
                mixed = weight_ref[c] * weighted[0]
                for h in range(1, channels):
                    mixed = mixed + weight_ref[h * fields + c] * weighted[h]
                out_ref[j, c] = out_ref[j, c] + mixed.astype(jnp.bfloat16).astype(jnp.float32)


def residual_sums(spread, innov, index, valid, scale, channel_weights):
    tiles, fields = spread.shape[0], spread.shape[1]
    owners, channels = innov.shape[0], innov.shape[1]
    smem = pl.BlockSpec(memory_space=pltpu.SMEM)
    return pl.pallas_call(
        residual_kernel,
        grid=(owners // OWNERS_STEP,),
        in_specs=[
            smem,
            smem,
            smem,
            smem,
            pl.BlockSpec(spread.shape, lambda s: (0, 0, 0, 0)),
            pl.BlockSpec((OWNERS_STEP,) + innov.shape[1:], lambda s: (s, 0, 0, 0)),
        ],
        out_specs=pl.BlockSpec(spread.shape, lambda s: (0, 0, 0, 0)),
        out_shape=jax.ShapeDtypeStruct(spread.shape, jnp.float32),
        scratch_shapes=[pltpu.VMEM((tiles, channels) + spread.shape[2:], jnp.float32)],
        compiler_params=pltpu.CompilerParams(dimension_semantics=("arbitrary",)),
    )(index, valid, scale, channel_weights.reshape(-1), spread, innov)


def observe(state, track_row, innov_row, weight_row, footprint, channel_weights):
    tiles = to_tiles(state).astype(jnp.bfloat16)
    spread = jnp.einsum("jcab,bd->jcad", tiles, footprint, preferred_element_type=jnp.float32)
    index = jnp.clip(track_row, 0, tiles.shape[0] - 1).astype(jnp.int32)
    valid = (track_row >= 0).astype(jnp.int32)
    scale = weight_row.astype(jnp.float32)
    summed = residual_sums(spread, innov_row, index, valid, scale, channel_weights)
    forcing = jnp.einsum(
        "tcad,bd->tcab", summed, footprint.astype(jnp.float32), precision=lax.Precision.HIGHEST
    )
    return from_tiles(forcing, state.shape[1], state.shape[2])


def on_device(
    increment,
    depth_field,
    coriolis,
    footprint,
    channel_weights,
    track_tiles,
    innovations,
    obs_weights,
):
    interval = STEPS // OBS_TIMES
    rows, cols = depth_field.shape
    band = lax.axis_index("lat")
    lat_total = cols * lax.axis_size("lat")

    innov = {
        t: lax.all_to_all(innovations[t, 0, 0], "lon", split_axis=0, concat_axis=0, tiled=True)
        for t in range(OBS_TIMES - 1, -1, -1)
    }
    gathered = lax.all_gather(obs_weights[:, 0, 0], "lon", axis=0)
    weights = lax.dynamic_index_in_dim(gathered, lax.axis_index("lon"), axis=2, keepdims=False)
    weights = weights.T
    tracks = track_tiles[:, 0, 0]

    lat_global = band * cols - HALO + jnp.arange(cols + 2 * HALO, dtype=jnp.int32)
    inside = ((lat_global >= 0) & (lat_global < lat_total))[None, :]
    cor = extend_lat(coriolis[None, :], HALO)

    fields = extend(jnp.concatenate([increment, depth_field[None]], axis=0), HALO)
    east_wind, north_wind, height, depth = fields[0], fields[1], fields[2], fields[3]
    inner = (slice(HALO, HALO + rows), slice(HALO, HALO + cols))

    forcings = []
    for step_index in range(STEPS):
        east_wind, north_wind, height = tangent_step(
            east_wind, north_wind, height, depth, cor, inside
        )
        if (step_index + 1) % interval == 0:
            obs_index = (step_index + 1) // interval - 1
            state = jnp.stack([east_wind[inner], north_wind[inner], height[inner]])
            forcing = observe(
                state,
                tracks[obs_index],
                innov[obs_index],
                weights[obs_index],
                footprint,
                channel_weights,
            )
            forcings.append(extend(forcing, HALO))

    east_adj = jnp.zeros_like(depth)
    north_adj = jnp.zeros_like(depth)
    height_adj = jnp.zeros_like(depth)
    for step_index in range(STEPS, 0, -1):
        if step_index % interval == 0:
            forcing = forcings[step_index // interval - 1]
            east_adj = east_adj + forcing[0]
            north_adj = north_adj + forcing[1]
            height_adj = height_adj + forcing[2]
        east_adj, north_adj, height_adj = adjoint_step(
            east_adj, north_adj, height_adj, depth, cor, inside
        )
    adjoint = jnp.stack([east_adj[inner], north_adj[inner], height_adj[inner]])
    return increment + adjoint


def solution(mesh):
    return jax.shard_map(
        on_device,
        mesh=mesh,
        in_specs=(
            P(None, "lon", "lat"),
            P("lon", "lat"),
            P("lat"),
            P(),
            P(),
            P(None, "lat", "lon", None),
            P(None, "lat", "lon", None, None, None, None),
            P(None, "lat", "lon", None),
        ),
        out_specs=P(None, "lon", "lat"),
        check_vma=False,
    )
```

```python
import jax
import jax.numpy as jnp
from jax import lax
from jax.sharding import PartitionSpec as P
from jax.experimental import pallas as pl
from jax.experimental.pallas import tpu as pltpu

TILE = 128
STEPS = 6
OBS_TIMES = 2
HALO = 2 * STEPS
OWNERS_STEP = 4


COURANT = 0.7


def extend_lon(x, width):
    peers, length = lax.axis_size("lon"), x.shape[-2]
    up = [(i, (i + 1) % peers) for i in range(peers)]
    down = [(j, i) for i, j in up]
    before = lax.ppermute(x[..., length - width :, :], "lon", up)
    after = lax.ppermute(x[..., :width, :], "lon", down)
    return jnp.concatenate([before, x, after], axis=-2)


def extend_lat(x, width):
    peers, length = lax.axis_size("lat"), x.shape[-1]
    up = [(i, i + 1) for i in range(peers - 1)]
    down = [(j, i) for i, j in up]
    before = lax.ppermute(x[..., length - width :], "lat", up)
    after = lax.ppermute(x[..., :width], "lat", down)
    return jnp.concatenate([before, x, after], axis=-1)


def extend(x, width):
    lon_peers, lat_peers = lax.axis_size("lon"), lax.axis_size("lat")
    rows, cols = x.shape[-2], x.shape[-1]
    lon_up = [(i, (i + 1) % lon_peers) for i in range(lon_peers)]
    lon_down = [(j, i) for i, j in lon_up]
    lat_up = [(i, i + 1) for i in range(lat_peers - 1)]
    lat_down = [(j, i) for i, j in lat_up]

    def both(lon_pairs, lat_pairs):
        return [
            (a * lat_peers + c, b * lat_peers + d) for a, b in lon_pairs for c, d in lat_pairs
        ]

    top, bottom = x[..., rows - width :, :], x[..., :width, :]
    before = lax.ppermute(top, "lon", lon_up)
    after = lax.ppermute(bottom, "lon", lon_down)
    left = lax.ppermute(x[..., cols - width :], "lat", lat_up)
    right = lax.ppermute(x[..., :width], "lat", lat_down)
    axes = ("lon", "lat")
    before_left = lax.ppermute(top[..., cols - width :], axes, both(lon_up, lat_up))
    before_right = lax.ppermute(top[..., :width], axes, both(lon_up, lat_down))
    after_left = lax.ppermute(bottom[..., cols - width :], axes, both(lon_down, lat_up))
    after_right = lax.ppermute(bottom[..., :width], axes, both(lon_down, lat_down))
    upper = jnp.concatenate([before_left, before, before_right], axis=-1)
    middle = jnp.concatenate([left, x, right], axis=-1)
    lower = jnp.concatenate([after_left, after, after_right], axis=-1)
    return jnp.concatenate([upper, middle, lower], axis=-2)


def extend_staged(x, width):
    return extend_lat(extend_lon(x, width), width)


def lon_diff(values):
    return 0.5 * (jnp.roll(values, -1, axis=0) - jnp.roll(values, 1, axis=0))


def lat_diff(values):
    return 0.5 * (jnp.roll(values, -1, axis=1) - jnp.roll(values, 1, axis=1))


def tangent_step(east_wind, north_wind, height, depth_field, coriolis, inside):
    height_next = height - COURANT * (
        lon_diff(depth_field * east_wind) + lat_diff(depth_field * north_wind)
    )
    height_next = jnp.where(inside, height_next, 0.0)
    east_next = east_wind + coriolis * north_wind - COURANT * lon_diff(height_next)
    north_next = north_wind - coriolis * east_next - COURANT * lat_diff(height_next)
    north_next = jnp.where(inside, north_next, 0.0)
    return (east_next, north_next, height_next)


def adjoint_step(east_adj, north_adj, height_adj, depth_field, coriolis, inside):
    east_once = east_adj - coriolis * north_adj
    height_once = height_adj + COURANT * (lat_diff(north_adj) + lon_diff(east_once))
    height_once = jnp.where(inside, height_once, 0.0)
    east_prev = east_once + COURANT * depth_field * lon_diff(height_once)
    north_prev = north_adj + coriolis * east_once + COURANT * depth_field * lat_diff(height_once)
    north_prev = jnp.where(inside, north_prev, 0.0)
    return (east_prev, north_prev, height_once)


def to_tiles(block_data):
    fields, row_total, col_total = block_data.shape
    blocks = block_data.reshape(fields, row_total // TILE, TILE, col_total // TILE, TILE)
    return blocks.transpose(1, 3, 0, 2, 4).reshape(-1, fields, TILE, TILE)


def from_tiles(pieces, row_total, col_total):
    fields = pieces.shape[1]
    blocks = pieces.reshape(row_total // TILE, col_total // TILE, fields, TILE, TILE)
    return blocks.transpose(2, 0, 3, 1, 4).reshape(fields, row_total, col_total)


def residual_kernel(index_ref, valid_ref, scale_ref, weight_ref, spread_ref, innov_ref, out_ref, radiance_ref):
    step = pl.program_id(0)
    tiles, fields = spread_ref.shape[0], spread_ref.shape[1]
    channels = radiance_ref.shape[1]

    @pl.when(step == 0)
    def _():
        for j in range(tiles):
            for h in range(channels):
                acc = weight_ref[h * fields] * spread_ref[j, 0]
                for c in range(1, fields):
                    acc = acc + weight_ref[h * fields + c] * spread_ref[j, c]
                radiance_ref[j, h] = acc
        out_ref[...] = jnp.zeros_like(out_ref)

    for k in range(OWNERS_STEP):
        owner = step * OWNERS_STEP + k
        j = index_ref[owner]
        scale = scale_ref[owner]

        @pl.when(valid_ref[owner] != 0)
        def _():
            weighted = [
                scale * (radiance_ref[j, h] - innov_ref[k, h].astype(jnp.float32))
                for h in range(channels)
            ]
            for c in range(fields):
                mixed = weight_ref[c] * weighted[0]
                for h in range(1, channels):
                    mixed = mixed + weight_ref[h * fields + c] * weighted[h]
                out_ref[j, c] = out_ref[j, c] + mixed.astype(jnp.bfloat16).astype(jnp.float32)


def residual_sums(spread, innov, index, valid, scale, channel_weights):
    tiles, fields = spread.shape[0], spread.shape[1]
    owners, channels = innov.shape[0], innov.shape[1]
    smem = pl.BlockSpec(memory_space=pltpu.SMEM)
    return pl.pallas_call(
        residual_kernel,
        grid=(owners // OWNERS_STEP,),
        in_specs=[
            smem,
            smem,
            smem,
            smem,
            pl.BlockSpec(spread.shape, lambda s: (0, 0, 0, 0)),
            pl.BlockSpec((OWNERS_STEP,) + innov.shape[1:], lambda s: (s, 0, 0, 0)),
        ],
        out_specs=pl.BlockSpec(spread.shape, lambda s: (0, 0, 0, 0)),
        out_shape=jax.ShapeDtypeStruct(spread.shape, jnp.float32),
        scratch_shapes=[pltpu.VMEM((tiles, channels) + spread.shape[2:], jnp.float32)],
        compiler_params=pltpu.CompilerParams(dimension_semantics=("arbitrary",)),
    )(index, valid, scale, channel_weights.reshape(-1), spread, innov)


def observe(state, track_row, innov_row, weight_row, footprint, channel_weights):
    tiles = to_tiles(state).astype(jnp.bfloat16)
    spread = jnp.einsum("jcab,bd->jcad", tiles, footprint, preferred_element_type=jnp.float32)
    index = jnp.clip(track_row, 0, tiles.shape[0] - 1).astype(jnp.int32)
    valid = (track_row >= 0).astype(jnp.int32)
    scale = weight_row.astype(jnp.float32)
    summed = residual_sums(spread, innov_row, index, valid, scale, channel_weights)
    forcing = jnp.einsum(
        "tcad,bd->tcab", summed, footprint.astype(jnp.float32), precision=lax.Precision.HIGHEST
    )
    return from_tiles(forcing, state.shape[1], state.shape[2])


def on_device(
    increment,
    depth_field,
    coriolis,
    footprint,
    channel_weights,
    track_tiles,
    innovations,
    obs_weights,
):
    interval = STEPS // OBS_TIMES
    rows, cols = depth_field.shape
    band = lax.axis_index("lat")
    lat_total = cols * lax.axis_size("lat")

    innov = [
        lax.all_to_all(innovations[t, 0, 0], "lon", split_axis=0, concat_axis=0, tiled=True)
        for t in range(OBS_TIMES - 1, -1, -1)
    ][::-1]
    weights = obs_weights[:, 0, 0]
    weights = lax.all_to_all(weights, "lon", split_axis=1, concat_axis=1, tiled=True)
    tracks = track_tiles[:, 0, 0]

    lat_global = band * cols - HALO + jnp.arange(cols + 2 * HALO, dtype=jnp.int32)
    inside = ((lat_global >= 0) & (lat_global < lat_total))[None, :]
    cor = extend_lat(coriolis[None, :], HALO)

    fields = extend(jnp.concatenate([increment, depth_field[None]], axis=0), HALO)
    east_wind, north_wind, height, depth = fields[0], fields[1], fields[2], fields[3]
    inner = (slice(HALO, HALO + rows), slice(HALO, HALO + cols))

    forcings = []
    for step_index in range(STEPS):
        east_wind, north_wind, height = tangent_step(
            east_wind, north_wind, height, depth, cor, inside
        )
        if (step_index + 1) % interval == 0:
            obs_index = (step_index + 1) // interval - 1
            state = jnp.stack([east_wind[inner], north_wind[inner], height[inner]])
            forcing = observe(
                state,
                tracks[obs_index],
                innov[obs_index],
                weights[obs_index],
                footprint,
                channel_weights,
            )
            forcings.append(extend(forcing, HALO))

    east_adj = jnp.zeros_like(depth)
    north_adj = jnp.zeros_like(depth)
    height_adj = jnp.zeros_like(depth)
    for step_index in range(STEPS, 0, -1):
        if step_index % interval == 0:
            forcing = forcings[step_index // interval - 1]
            east_adj = east_adj + forcing[0]
            north_adj = north_adj + forcing[1]
            height_adj = height_adj + forcing[2]
        east_adj, north_adj, height_adj = adjoint_step(
            east_adj, north_adj, height_adj, depth, cor, inside
        )
    adjoint = jnp.stack([east_adj[inner], north_adj[inner], height_adj[inner]])
    return increment + adjoint


def solution(mesh):
    return jax.shard_map(
        on_device,
        mesh=mesh,
        in_specs=(
            P(None, "lon", "lat"),
            P("lon", "lat"),
            P("lat"),
            P(),
            P(),
            P(None, "lat", "lon", None),
            P(None, "lat", "lon", None, None, None, None),
            P(None, "lat", "lon", None),
        ),
        out_specs=P(None, "lon", "lat"),
        check_vma=False,
    )
```

```python
import jax
import jax.numpy as jnp
from jax import lax
from jax.sharding import PartitionSpec as P
from jax.experimental import pallas as pl
from jax.experimental.pallas import tpu as pltpu

TILE = 128
STEPS = 6
OBS_TIMES = 2
HALO = 2 * STEPS
OWNERS_STEP = 4


COURANT = 0.7


def extend_lon(x, width):
    peers, length = lax.axis_size("lon"), x.shape[-2]
    up = [(i, (i + 1) % peers) for i in range(peers)]
    down = [(j, i) for i, j in up]
    before = lax.ppermute(x[..., length - width :, :], "lon", up)
    after = lax.ppermute(x[..., :width, :], "lon", down)
    return jnp.concatenate([before, x, after], axis=-2)


def extend_lat(x, width):
    peers, length = lax.axis_size("lat"), x.shape[-1]
    up = [(i, i + 1) for i in range(peers - 1)]
    down = [(j, i) for i, j in up]
    before = lax.ppermute(x[..., length - width :], "lat", up)
    after = lax.ppermute(x[..., :width], "lat", down)
    return jnp.concatenate([before, x, after], axis=-1)


def extend(x, width):
    return extend_lat(extend_lon(x, width), width)


def lon_diff(values):
    return 0.5 * (jnp.roll(values, -1, axis=0) - jnp.roll(values, 1, axis=0))


def lat_diff(values):
    return 0.5 * (jnp.roll(values, -1, axis=1) - jnp.roll(values, 1, axis=1))


def tangent_step(east_wind, north_wind, height, depth_field, coriolis, inside):
    height_next = height - COURANT * (
        lon_diff(depth_field * east_wind) + lat_diff(depth_field * north_wind)
    )
    height_next = jnp.where(inside, height_next, 0.0)
    east_next = east_wind + coriolis * north_wind - COURANT * lon_diff(height_next)
    north_next = north_wind - coriolis * east_next - COURANT * lat_diff(height_next)
    north_next = jnp.where(inside, north_next, 0.0)
    return (east_next, north_next, height_next)


def adjoint_step(east_adj, north_adj, height_adj, depth_field, coriolis, inside):
    east_once = east_adj - coriolis * north_adj
    height_once = height_adj + COURANT * (lat_diff(north_adj) + lon_diff(east_once))
    height_once = jnp.where(inside, height_once, 0.0)
    east_prev = east_once + COURANT * depth_field * lon_diff(height_once)
    north_prev = north_adj + coriolis * east_once + COURANT * depth_field * lat_diff(height_once)
    north_prev = jnp.where(inside, north_prev, 0.0)
    return (east_prev, north_prev, height_once)


def to_tiles(block_data):
    fields, row_total, col_total = block_data.shape
    blocks = block_data.reshape(fields, row_total // TILE, TILE, col_total // TILE, TILE)
    return blocks.transpose(1, 3, 0, 2, 4).reshape(-1, fields, TILE, TILE)


def from_tiles(pieces, row_total, col_total):
    fields = pieces.shape[1]
    blocks = pieces.reshape(row_total // TILE, col_total // TILE, fields, TILE, TILE)
    return blocks.transpose(2, 0, 3, 1, 4).reshape(fields, row_total, col_total)


def residual_kernel(index_ref, valid_ref, scale_ref, weight_ref, spread_ref, innov_ref, out_ref, radiance_ref):
    step = pl.program_id(0)
    tiles, fields = spread_ref.shape[0], spread_ref.shape[1]
    channels = radiance_ref.shape[1]

    @pl.when(step == 0)
    def _():
        for j in range(tiles):
            for h in range(channels):
                acc = weight_ref[h * fields] * spread_ref[j, 0]
                for c in range(1, fields):
                    acc = acc + weight_ref[h * fields + c] * spread_ref[j, c]
                radiance_ref[j, h] = acc
        out_ref[...] = jnp.zeros_like(out_ref)

    for k in range(OWNERS_STEP):
        owner = step * OWNERS_STEP + k
        j = index_ref[owner]
        scale = scale_ref[owner]

        @pl.when(valid_ref[owner] != 0)
        def _():
            weighted = [
                scale * (radiance_ref[j, h] - innov_ref[k, h].astype(jnp.float32))
                for h in range(channels)
            ]
            for c in range(fields):
                mixed = weight_ref[c] * weighted[0]
                for h in range(1, channels):
                    mixed = mixed + weight_ref[h * fields + c] * weighted[h]
                out_ref[j, c] = out_ref[j, c] + mixed.astype(jnp.bfloat16).astype(jnp.float32)


def residual_sums(spread, innov, index, valid, scale, channel_weights):
    tiles, fields = spread.shape[0], spread.shape[1]
    owners, channels = innov.shape[0], innov.shape[1]
    smem = pl.BlockSpec(memory_space=pltpu.SMEM)
    return pl.pallas_call(
        residual_kernel,
        grid=(owners // OWNERS_STEP,),
        in_specs=[
            smem,
            smem,
            smem,
            smem,
            pl.BlockSpec(spread.shape, lambda s: (0, 0, 0, 0)),
            pl.BlockSpec((OWNERS_STEP,) + innov.shape[1:], lambda s: (s, 0, 0, 0)),
        ],
        out_specs=pl.BlockSpec(spread.shape, lambda s: (0, 0, 0, 0)),
        out_shape=jax.ShapeDtypeStruct(spread.shape, jnp.float32),
        scratch_shapes=[pltpu.VMEM((tiles, channels) + spread.shape[2:], jnp.float32)],
        compiler_params=pltpu.CompilerParams(dimension_semantics=("arbitrary",)),
    )(index, valid, scale, channel_weights.reshape(-1), spread, innov)


def observe(state, track_row, innov_row, weight_row, footprint, channel_weights):
    tiles = to_tiles(state).astype(jnp.bfloat16)
    spread = jnp.einsum("jcab,bd->jcad", tiles, footprint, preferred_element_type=jnp.float32)
    index = jnp.clip(track_row, 0, tiles.shape[0] - 1).astype(jnp.int32)
    valid = (track_row >= 0).astype(jnp.int32)
    scale = weight_row.astype(jnp.float32)
    summed = residual_sums(spread, innov_row, index, valid, scale, channel_weights)
    forcing = jnp.einsum(
        "tcad,bd->tcab", summed, footprint.astype(jnp.float32), precision=lax.Precision.HIGHEST
    )
    return from_tiles(forcing, state.shape[1], state.shape[2])


def on_device(
    increment,
    depth_field,
    coriolis,
    footprint,
    channel_weights,
    track_tiles,
    innovations,
    obs_weights,
):
    interval = STEPS // OBS_TIMES
    rows, cols = depth_field.shape
    band = lax.axis_index("lat")
    lat_total = cols * lax.axis_size("lat")

    innov = [
        lax.all_to_all(innovations[t, 0, 0], "lon", split_axis=0, concat_axis=0, tiled=True)
        for t in range(OBS_TIMES)
    ]
    weights = obs_weights[:, 0, 0]
    weights = lax.all_to_all(weights, "lon", split_axis=1, concat_axis=1, tiled=True)
    tracks = track_tiles[:, 0, 0]

    lat_global = band * cols - HALO + jnp.arange(cols + 2 * HALO, dtype=jnp.int32)
    inside = ((lat_global >= 0) & (lat_global < lat_total))[None, :]
    cor = extend_lat(coriolis[None, :], HALO)

    fields = extend(jnp.concatenate([increment, depth_field[None]], axis=0), HALO)
    east_wind, north_wind, height, depth = fields[0], fields[1], fields[2], fields[3]
    inner = (slice(HALO, HALO + rows), slice(HALO, HALO + cols))

    def tangent_run(_, state):
        return tangent_step(*state, depth, cor, inside)

    def adjoint_run(_, state):
        return adjoint_step(*state, depth, cor, inside)

    state = (east_wind, north_wind, height)
    forcings = []
    for obs_index in range(OBS_TIMES):
        state = lax.fori_loop(0, interval, tangent_run, state)
        stacked = jnp.stack([field[inner] for field in state])
        forcing = observe(
            stacked,
            tracks[obs_index],
            innov[obs_index],
            weights[obs_index],
            footprint,
            channel_weights,
        )
        forcings.append(extend(forcing, HALO))

    state = (jnp.zeros_like(depth),) * 3
    for obs_index in range(OBS_TIMES - 1, -1, -1):
        state = tuple(field + forced for field, forced in zip(state, forcings[obs_index]))
        state = lax.fori_loop(0, interval, adjoint_run, state)
    east_adj, north_adj, height_adj = state
    adjoint = jnp.stack([east_adj[inner], north_adj[inner], height_adj[inner]])
    return increment + adjoint


def solution(mesh):
    return jax.shard_map(
        on_device,
        mesh=mesh,
        in_specs=(
            P(None, "lon", "lat"),
            P("lon", "lat"),
            P("lat"),
            P(),
            P(),
            P(None, "lat", "lon", None),
            P(None, "lat", "lon", None, None, None, None),
            P(None, "lat", "lon", None),
        ),
        out_specs=P(None, "lon", "lat"),
        check_vma=False,
    )
```

```python
import jax
import jax.numpy as jnp
from jax import lax
from jax.sharding import PartitionSpec as P
from jax.experimental import pallas as pl
from jax.experimental.pallas import tpu as pltpu

TILE = 128
STEPS = 6
OBS_TIMES = 2
HALO = 2 * STEPS
OWNERS_STEP = 4


COURANT = 0.7


def extend_lon(x, width):
    peers, length = lax.axis_size("lon"), x.shape[-2]
    up = [(i, (i + 1) % peers) for i in range(peers)]
    down = [(j, i) for i, j in up]
    before = lax.ppermute(x[..., length - width :, :], "lon", up)
    after = lax.ppermute(x[..., :width, :], "lon", down)
    return jnp.concatenate([before, x, after], axis=-2)


def extend_lat(x, width):
    peers, length = lax.axis_size("lat"), x.shape[-1]
    up = [(i, i + 1) for i in range(peers - 1)]
    down = [(j, i) for i, j in up]
    before = lax.ppermute(x[..., length - width :], "lat", up)
    after = lax.ppermute(x[..., :width], "lat", down)
    return jnp.concatenate([before, x, after], axis=-1)


def extend(x, width):
    return extend_lat(extend_lon(x, width), width)


def lon_diff(values):
    return 0.5 * (jnp.roll(values, -1, axis=0) - jnp.roll(values, 1, axis=0))


def lat_diff(values):
    return 0.5 * (jnp.roll(values, -1, axis=1) - jnp.roll(values, 1, axis=1))


def tangent_step(east_wind, north_wind, height, depth_field, coriolis, inside):
    height_next = height - COURANT * (
        lon_diff(depth_field * east_wind) + lat_diff(depth_field * north_wind)
    )
    height_next = jnp.where(inside, height_next, 0.0)
    east_next = east_wind + coriolis * north_wind - COURANT * lon_diff(height_next)
    north_next = north_wind - coriolis * east_next - COURANT * lat_diff(height_next)
    north_next = jnp.where(inside, north_next, 0.0)
    return (east_next, north_next, height_next)


def adjoint_step(east_adj, north_adj, height_adj, depth_field, coriolis, inside):
    east_once = east_adj - coriolis * north_adj
    height_once = height_adj + COURANT * (lat_diff(north_adj) + lon_diff(east_once))
    height_once = jnp.where(inside, height_once, 0.0)
    east_prev = east_once + COURANT * depth_field * lon_diff(height_once)
    north_prev = north_adj + coriolis * east_once + COURANT * depth_field * lat_diff(height_once)
    north_prev = jnp.where(inside, north_prev, 0.0)
    return (east_prev, north_prev, height_once)


def to_tiles(block_data):
    fields, row_total, col_total = block_data.shape
    blocks = block_data.reshape(fields, row_total // TILE, TILE, col_total // TILE, TILE)
    return blocks.transpose(1, 3, 0, 2, 4).reshape(-1, fields, TILE, TILE)


def from_tiles(pieces, row_total, col_total):
    fields = pieces.shape[1]
    blocks = pieces.reshape(row_total // TILE, col_total // TILE, fields, TILE, TILE)
    return blocks.transpose(2, 0, 3, 1, 4).reshape(fields, row_total, col_total)


def residual_kernel(index_ref, valid_ref, scale_ref, weight_ref, spread_ref, innov_ref, out_ref, radiance_ref):
    step = pl.program_id(0)
    tiles, fields = spread_ref.shape[0], spread_ref.shape[1]
    channels = radiance_ref.shape[1]

    @pl.when(step == 0)
    def _():
        for j in range(tiles):
            for h in range(channels):
                acc = weight_ref[h * fields] * spread_ref[j, 0]
                for c in range(1, fields):
                    acc = acc + weight_ref[h * fields + c] * spread_ref[j, c]
                radiance_ref[j, h] = acc
        out_ref[...] = jnp.zeros_like(out_ref)

    for k in range(OWNERS_STEP):
        owner = step * OWNERS_STEP + k
        j = index_ref[owner]
        scale = scale_ref[owner]

        @pl.when(valid_ref[owner] != 0)
        def _():
            weighted = [
                scale
                * (
                    radiance_ref[j, h]
                    - innov_ref[k, h * TILE : (h + 1) * TILE, :].astype(jnp.float32)
                )
                for h in range(channels)
            ]
            for c in range(fields):
                mixed = weight_ref[c] * weighted[0]
                for h in range(1, channels):
                    mixed = mixed + weight_ref[h * fields + c] * weighted[h]
                out_ref[j, c] = out_ref[j, c] + mixed.astype(jnp.bfloat16).astype(jnp.float32)


def residual_sums(spread, innov, index, valid, scale, channel_weights):
    tiles, fields = spread.shape[0], spread.shape[1]
    owners, channels = innov.shape[0], channel_weights.shape[0]
    smem = pl.BlockSpec(memory_space=pltpu.SMEM)
    return pl.pallas_call(
        residual_kernel,
        grid=(owners // OWNERS_STEP,),
        in_specs=[
            smem,
            smem,
            smem,
            smem,
            pl.BlockSpec(spread.shape, lambda s: (0, 0, 0, 0)),
            pl.BlockSpec((OWNERS_STEP,) + innov.shape[1:], lambda s: (s, 0, 0)),
        ],
        out_specs=pl.BlockSpec(spread.shape, lambda s: (0, 0, 0, 0)),
        out_shape=jax.ShapeDtypeStruct(spread.shape, jnp.float32),
        scratch_shapes=[pltpu.VMEM((tiles, channels) + spread.shape[2:], jnp.float32)],
        compiler_params=pltpu.CompilerParams(dimension_semantics=("arbitrary",)),
    )(index, valid, scale, channel_weights.reshape(-1), spread, innov)


def observe(state, track_row, innov_row, weight_row, footprint, channel_weights):
    tiles = to_tiles(state).astype(jnp.bfloat16)
    spread = jnp.einsum("jcab,bd->jcad", tiles, footprint, preferred_element_type=jnp.float32)
    index = jnp.clip(track_row, 0, tiles.shape[0] - 1).astype(jnp.int32)
    valid = (track_row >= 0).astype(jnp.int32)
    scale = weight_row.astype(jnp.float32)
    summed = residual_sums(spread, innov_row, index, valid, scale, channel_weights)
    forcing = jnp.einsum(
        "tcad,bd->tcab", summed, footprint.astype(jnp.float32), precision=lax.Precision.HIGHEST
    )
    return from_tiles(forcing, state.shape[1], state.shape[2])


def on_device(
    increment,
    depth_field,
    coriolis,
    footprint,
    channel_weights,
    track_tiles,
    innovations,
    obs_weights,
):
    interval = STEPS // OBS_TIMES
    rows, cols = depth_field.shape
    band = lax.axis_index("lat")
    lat_total = cols * lax.axis_size("lat")

    owners, channels = innovations.shape[3], innovations.shape[4]
    innov, weights = [], []
    for t in range(OBS_TIMES):
        extra = jnp.zeros((owners, 1, TILE), innovations.dtype)
        extra = extra.at[:, 0, 0].set(obs_weights[t, 0, 0])
        packed = jnp.concatenate(
            [innovations[t, 0, 0].reshape(owners, channels * TILE, TILE), extra], axis=1
        )
        packed = lax.all_to_all(packed, "lon", split_axis=0, concat_axis=0, tiled=True)
        innov.append(packed)
        weights.append(packed[:, channels * TILE, 0])
    tracks = track_tiles[:, 0, 0]

    lat_global = band * cols - HALO + jnp.arange(cols + 2 * HALO, dtype=jnp.int32)
    inside = ((lat_global >= 0) & (lat_global < lat_total))[None, :]
    cor = extend_lat(coriolis[None, :], HALO)

    fields = extend(jnp.concatenate([increment, depth_field[None]], axis=0), HALO)
    east_wind, north_wind, height, depth = fields[0], fields[1], fields[2], fields[3]
    inner = (slice(HALO, HALO + rows), slice(HALO, HALO + cols))

    def tangent_run(_, state):
        return tangent_step(*state, depth, cor, inside)

    def adjoint_run(_, state):
        return adjoint_step(*state, depth, cor, inside)

    state = (east_wind, north_wind, height)
    forcings = []
    for obs_index in range(OBS_TIMES):
        state = lax.fori_loop(0, interval, tangent_run, state)
        stacked = jnp.stack([field[inner] for field in state])
        forcing = observe(
            stacked,
            tracks[obs_index],
            innov[obs_index],
            weights[obs_index],
            footprint,
            channel_weights,
        )
        forcings.append(extend(forcing, HALO))

    state = (jnp.zeros_like(depth),) * 3
    for obs_index in range(OBS_TIMES - 1, -1, -1):
        state = tuple(field + forced for field, forced in zip(state, forcings[obs_index]))
        state = lax.fori_loop(0, interval, adjoint_run, state)
    east_adj, north_adj, height_adj = state
    adjoint = jnp.stack([east_adj[inner], north_adj[inner], height_adj[inner]])
    return increment + adjoint


def solution(mesh):
    return jax.shard_map(
        on_device,
        mesh=mesh,
        in_specs=(
            P(None, "lon", "lat"),
            P("lon", "lat"),
            P("lat"),
            P(),
            P(),
            P(None, "lat", "lon", None),
            P(None, "lat", "lon", None, None, None, None),
            P(None, "lat", "lon", None),
        ),
        out_specs=P(None, "lon", "lat"),
        check_vma=False,
    )
```

```python
import jax
import jax.numpy as jnp
from jax import lax
from jax.sharding import PartitionSpec as P
from jax.experimental import pallas as pl
from jax.experimental.pallas import tpu as pltpu

TILE = 128
STEPS = 6
OBS_TIMES = 2
HALO = 2 * STEPS
OWNERS_STEP = 4


COURANT = 0.7


def extend_lon(x, width):
    peers, length = lax.axis_size("lon"), x.shape[-2]
    up = [(i, (i + 1) % peers) for i in range(peers)]
    down = [(j, i) for i, j in up]
    before = lax.ppermute(x[..., length - width :, :], "lon", up)
    after = lax.ppermute(x[..., :width, :], "lon", down)
    return jnp.concatenate([before, x, after], axis=-2)


def extend_lat(x, width):
    peers, length = lax.axis_size("lat"), x.shape[-1]
    up = [(i, i + 1) for i in range(peers - 1)]
    down = [(j, i) for i, j in up]
    before = lax.ppermute(x[..., length - width :], "lat", up)
    after = lax.ppermute(x[..., :width], "lat", down)
    return jnp.concatenate([before, x, after], axis=-1)


def extend(x, width):
    return extend_lat(extend_lon(x, width), width)


def lon_diff(values):
    return 0.5 * (jnp.roll(values, -1, axis=0) - jnp.roll(values, 1, axis=0))


def lat_diff(values):
    return 0.5 * (jnp.roll(values, -1, axis=1) - jnp.roll(values, 1, axis=1))


def tangent_step(east_wind, north_wind, height, depth_field, coriolis, inside):
    height_next = height - COURANT * (
        lon_diff(depth_field * east_wind) + lat_diff(depth_field * north_wind)
    )
    height_next = jnp.where(inside, height_next, 0.0)
    east_next = east_wind + coriolis * north_wind - COURANT * lon_diff(height_next)
    north_next = north_wind - coriolis * east_next - COURANT * lat_diff(height_next)
    north_next = jnp.where(inside, north_next, 0.0)
    return (east_next, north_next, height_next)


def adjoint_step(east_adj, north_adj, height_adj, depth_field, coriolis, inside):
    east_once = east_adj - coriolis * north_adj
    height_once = height_adj + COURANT * (lat_diff(north_adj) + lon_diff(east_once))
    height_once = jnp.where(inside, height_once, 0.0)
    east_prev = east_once + COURANT * depth_field * lon_diff(height_once)
    north_prev = north_adj + coriolis * east_once + COURANT * depth_field * lat_diff(height_once)
    north_prev = jnp.where(inside, north_prev, 0.0)
    return (east_prev, north_prev, height_once)


def to_tiles(block_data):
    fields, row_total, col_total = block_data.shape
    blocks = block_data.reshape(fields, row_total // TILE, TILE, col_total // TILE, TILE)
    return blocks.transpose(1, 3, 0, 2, 4).reshape(-1, fields, TILE, TILE)


def from_tiles(pieces, row_total, col_total):
    fields = pieces.shape[1]
    blocks = pieces.reshape(row_total // TILE, col_total // TILE, fields, TILE, TILE)
    return blocks.transpose(2, 0, 3, 1, 4).reshape(fields, row_total, col_total)


def residual_kernel(index_ref, valid_ref, scale_ref, weight_ref, spread_ref, innov_ref, out_ref, radiance_ref):
    step = pl.program_id(0)
    tiles, fields = spread_ref.shape[0], spread_ref.shape[1]
    channels = radiance_ref.shape[1]

    @pl.when(step == 0)
    def _():
        for j in range(tiles):
            for h in range(channels):
                acc = weight_ref[h * fields] * spread_ref[j, 0]
                for c in range(1, fields):
                    acc = acc + weight_ref[h * fields + c] * spread_ref[j, c]
                radiance_ref[j, h] = acc
        out_ref[...] = jnp.zeros_like(out_ref)

    for k in range(OWNERS_STEP):
        owner = step * OWNERS_STEP + k
        j = index_ref[owner]
        scale = scale_ref[owner]

        @pl.when(valid_ref[owner] != 0)
        def _():
            weighted = [
                scale
                * (
                    radiance_ref[j, h]
                    - innov_ref[k, h * TILE : (h + 1) * TILE, :].astype(jnp.float32)
                )
                for h in range(channels)
            ]
            for c in range(fields):
                mixed = weight_ref[c] * weighted[0]
                for h in range(1, channels):
                    mixed = mixed + weight_ref[h * fields + c] * weighted[h]
                out_ref[j, c] = out_ref[j, c] + mixed.astype(jnp.bfloat16).astype(jnp.float32)


def residual_sums(spread, innov, index, valid, scale, channel_weights):
    tiles, fields = spread.shape[0], spread.shape[1]
    owners, channels = innov.shape[0], channel_weights.shape[0]
    smem = pl.BlockSpec(memory_space=pltpu.SMEM)
    return pl.pallas_call(
        residual_kernel,
        grid=(owners // OWNERS_STEP,),
        in_specs=[
            smem,
            smem,
            smem,
            smem,
            pl.BlockSpec(spread.shape, lambda s: (0, 0, 0, 0)),
            pl.BlockSpec((OWNERS_STEP,) + innov.shape[1:], lambda s: (s, 0, 0)),
        ],
        out_specs=pl.BlockSpec(spread.shape, lambda s: (0, 0, 0, 0)),
        out_shape=jax.ShapeDtypeStruct(spread.shape, jnp.float32),
        scratch_shapes=[pltpu.VMEM((tiles, channels) + spread.shape[2:], jnp.float32)],
        compiler_params=pltpu.CompilerParams(dimension_semantics=("arbitrary",)),
    )(index, valid, scale, channel_weights.reshape(-1), spread, innov)


def observe(state, track_row, innov_row, weight_row, footprint, channel_weights):
    tiles = to_tiles(state).astype(jnp.bfloat16)
    spread = jnp.einsum("jcab,bd->jcad", tiles, footprint, preferred_element_type=jnp.float32)
    index = jnp.clip(track_row, 0, tiles.shape[0] - 1).astype(jnp.int32)
    valid = (track_row >= 0).astype(jnp.int32)
    scale = weight_row.astype(jnp.float32)
    summed = residual_sums(spread, innov_row, index, valid, scale, channel_weights)
    forcing = jnp.einsum(
        "tcad,bd->tcab", summed, footprint.astype(jnp.float32), precision=lax.Precision.HIGHEST
    )
    return from_tiles(forcing, state.shape[1], state.shape[2])


def on_device(
    increment,
    depth_field,
    coriolis,
    footprint,
    channel_weights,
    track_tiles,
    innovations,
    obs_weights,
):
    interval = STEPS // OBS_TIMES
    rows, cols = depth_field.shape
    band = lax.axis_index("lat")
    lat_total = cols * lax.axis_size("lat")

    owners, channels = innovations.shape[3], innovations.shape[4]
    innov, weights = [], []
    for t in range(OBS_TIMES):
        extra = jnp.zeros((owners, 1, TILE), innovations.dtype)
        extra = extra.at[:, 0, 0].set(obs_weights[t, 0, 0])
        packed = jnp.concatenate(
            [innovations[t, 0, 0].reshape(owners, channels * TILE, TILE), extra], axis=1
        )
        innov.append(packed)
    tracks = track_tiles[:, 0, 0]

    lat_global = band * cols - HALO + jnp.arange(cols + 2 * HALO, dtype=jnp.int32)
    inside = ((lat_global >= 0) & (lat_global < lat_total))[None, :]
    cor = extend_lat(coriolis[None, :], HALO)

    fields = extend(jnp.concatenate([increment, depth_field[None]], axis=0), HALO)
    fields, innov = lax.optimization_barrier((fields, innov))
    innov = [
        lax.all_to_all(packed, "lon", split_axis=0, concat_axis=0, tiled=True) for packed in innov
    ]
    weights = [packed[:, channels * TILE, 0] for packed in innov]
    east_wind, north_wind, height, depth = fields[0], fields[1], fields[2], fields[3]
    inner = (slice(HALO, HALO + rows), slice(HALO, HALO + cols))

    def tangent_run(_, state):
        return tangent_step(*state, depth, cor, inside)

    def adjoint_run(_, state):
        return adjoint_step(*state, depth, cor, inside)

    state = (east_wind, north_wind, height)
    forcings = []
    for obs_index in range(OBS_TIMES):
        state = lax.fori_loop(0, interval, tangent_run, state)
        stacked = jnp.stack([field[inner] for field in state])
        forcing = observe(
            stacked,
            tracks[obs_index],
            innov[obs_index],
            weights[obs_index],
            footprint,
            channel_weights,
        )
        forcings.append(extend(forcing, HALO))

    state = (jnp.zeros_like(depth),) * 3
    for obs_index in range(OBS_TIMES - 1, -1, -1):
        state = tuple(field + forced for field, forced in zip(state, forcings[obs_index]))
        state = lax.fori_loop(0, interval, adjoint_run, state)
    east_adj, north_adj, height_adj = state
    adjoint = jnp.stack([east_adj[inner], north_adj[inner], height_adj[inner]])
    return increment + adjoint


def solution(mesh):
    return jax.shard_map(
        on_device,
        mesh=mesh,
        in_specs=(
            P(None, "lon", "lat"),
            P("lon", "lat"),
            P("lat"),
            P(),
            P(),
            P(None, "lat", "lon", None),
            P(None, "lat", "lon", None, None, None, None),
            P(None, "lat", "lon", None),
        ),
        out_specs=P(None, "lon", "lat"),
        check_vma=False,
    )
```

```python
import jax
import jax.numpy as jnp
from jax import lax
from jax.sharding import PartitionSpec as P
from jax.experimental import pallas as pl
from jax.experimental.pallas import tpu as pltpu

TILE = 128
STEPS = 6
OBS_TIMES = 2
HALO = 2 * STEPS
OWNERS_STEP = 8


COURANT = 0.7


def extend_lon(x, width):
    peers, length = lax.axis_size("lon"), x.shape[-2]
    up = [(i, (i + 1) % peers) for i in range(peers)]
    down = [(j, i) for i, j in up]
    before = lax.ppermute(x[..., length - width :, :], "lon", up)
    after = lax.ppermute(x[..., :width, :], "lon", down)
    return jnp.concatenate([before, x, after], axis=-2)


def extend_lat(x, width):
    peers, length = lax.axis_size("lat"), x.shape[-1]
    up = [(i, i + 1) for i in range(peers - 1)]
    down = [(j, i) for i, j in up]
    before = lax.ppermute(x[..., length - width :], "lat", up)
    after = lax.ppermute(x[..., :width], "lat", down)
    return jnp.concatenate([before, x, after], axis=-1)


def extend(x, width):
    return extend_lat(extend_lon(x, width), width)


def lon_diff(values):
    return 0.5 * (jnp.roll(values, -1, axis=0) - jnp.roll(values, 1, axis=0))


def lat_diff(values):
    return 0.5 * (jnp.roll(values, -1, axis=1) - jnp.roll(values, 1, axis=1))


def tangent_step(east_wind, north_wind, height, depth_field, coriolis, inside):
    height_next = height - COURANT * (
        lon_diff(depth_field * east_wind) + lat_diff(depth_field * north_wind)
    )
    height_next = jnp.where(inside, height_next, 0.0)
    east_next = east_wind + coriolis * north_wind - COURANT * lon_diff(height_next)
    north_next = north_wind - coriolis * east_next - COURANT * lat_diff(height_next)
    north_next = jnp.where(inside, north_next, 0.0)
    return (east_next, north_next, height_next)


def adjoint_step(east_adj, north_adj, height_adj, depth_field, coriolis, inside):
    east_once = east_adj - coriolis * north_adj
    height_once = height_adj + COURANT * (lat_diff(north_adj) + lon_diff(east_once))
    height_once = jnp.where(inside, height_once, 0.0)
    east_prev = east_once + COURANT * depth_field * lon_diff(height_once)
    north_prev = north_adj + coriolis * east_once + COURANT * depth_field * lat_diff(height_once)
    north_prev = jnp.where(inside, north_prev, 0.0)
    return (east_prev, north_prev, height_once)


def to_tiles(block_data):
    fields, row_total, col_total = block_data.shape
    blocks = block_data.reshape(fields, row_total // TILE, TILE, col_total // TILE, TILE)
    return blocks.transpose(1, 3, 0, 2, 4).reshape(-1, fields, TILE, TILE)


def from_tiles(pieces, row_total, col_total):
    fields = pieces.shape[1]
    blocks = pieces.reshape(row_total // TILE, col_total // TILE, fields, TILE, TILE)
    return blocks.transpose(2, 0, 3, 1, 4).reshape(fields, row_total, col_total)


def residual_kernel(index_ref, valid_ref, scale_ref, weight_ref, spread_ref, innov_ref, out_ref, radiance_ref):
    step = pl.program_id(0)
    tiles, fields = spread_ref.shape[0], spread_ref.shape[1]
    channels = radiance_ref.shape[1]

    @pl.when(step == 0)
    def _():
        for j in range(tiles):
            for h in range(channels):
                acc = weight_ref[h * fields] * spread_ref[j, 0]
                for c in range(1, fields):
                    acc = acc + weight_ref[h * fields + c] * spread_ref[j, c]
                radiance_ref[j, h] = acc
        out_ref[...] = jnp.zeros_like(out_ref)

    for k in range(OWNERS_STEP):
        owner = step * OWNERS_STEP + k
        j = index_ref[owner]
        scale = scale_ref[owner]

        @pl.when(valid_ref[owner] != 0)
        def _():
            weighted = [
                scale
                * (
                    radiance_ref[j, h]
                    - innov_ref[k, h * TILE : (h + 1) * TILE, :].astype(jnp.float32)
                )
                for h in range(channels)
            ]
            for c in range(fields):
                mixed = weight_ref[c] * weighted[0]
                for h in range(1, channels):
                    mixed = mixed + weight_ref[h * fields + c] * weighted[h]
                out_ref[j, c] = out_ref[j, c] + mixed.astype(jnp.bfloat16).astype(jnp.float32)


def residual_sums(spread, innov, index, valid, scale, channel_weights):
    tiles, fields = spread.shape[0], spread.shape[1]
    owners, channels = innov.shape[0], channel_weights.shape[0]
    smem = pl.BlockSpec(memory_space=pltpu.SMEM)
    return pl.pallas_call(
        residual_kernel,
        grid=(owners // OWNERS_STEP,),
        in_specs=[
            smem,
            smem,
            smem,
            smem,
            pl.BlockSpec(spread.shape, lambda s: (0, 0, 0, 0)),
            pl.BlockSpec((OWNERS_STEP,) + innov.shape[1:], lambda s: (s, 0, 0)),
        ],
        out_specs=pl.BlockSpec(spread.shape, lambda s: (0, 0, 0, 0)),
        out_shape=jax.ShapeDtypeStruct(spread.shape, jnp.float32),
        scratch_shapes=[pltpu.VMEM((tiles, channels) + spread.shape[2:], jnp.float32)],
        compiler_params=pltpu.CompilerParams(dimension_semantics=("arbitrary",)),
    )(index, valid, scale, channel_weights.reshape(-1), spread, innov)


def observe(state, track_row, innov_row, weight_row, footprint, channel_weights):
    tiles = to_tiles(state).astype(jnp.bfloat16)
    spread = jnp.einsum("jcab,bd->jcad", tiles, footprint, preferred_element_type=jnp.float32)
    index = jnp.clip(track_row, 0, tiles.shape[0] - 1).astype(jnp.int32)
    valid = (track_row >= 0).astype(jnp.int32)
    scale = weight_row.astype(jnp.float32)
    summed = residual_sums(spread, innov_row, index, valid, scale, channel_weights)
    forcing = jnp.einsum(
        "tcad,bd->tcab", summed, footprint.astype(jnp.float32), precision=lax.Precision.HIGHEST
    )
    return from_tiles(forcing, state.shape[1], state.shape[2])


def on_device(
    increment,
    depth_field,
    coriolis,
    footprint,
    channel_weights,
    track_tiles,
    innovations,
    obs_weights,
):
    interval = STEPS // OBS_TIMES
    rows, cols = depth_field.shape
    band = lax.axis_index("lat")
    lat_total = cols * lax.axis_size("lat")

    owners, channels = innovations.shape[3], innovations.shape[4]
    innov, weights = [], []
    for t in range(OBS_TIMES):
        extra = jnp.zeros((owners, 1, TILE), innovations.dtype)
        extra = extra.at[:, 0, 0].set(obs_weights[t, 0, 0])
        packed = jnp.concatenate(
            [innovations[t, 0, 0].reshape(owners, channels * TILE, TILE), extra], axis=1
        )
        packed = lax.all_to_all(packed, "lon", split_axis=0, concat_axis=0, tiled=True)
        innov.append(packed)
        weights.append(packed[:, channels * TILE, 0])
    tracks = track_tiles[:, 0, 0]

    lat_global = band * cols - HALO + jnp.arange(cols + 2 * HALO, dtype=jnp.int32)
    inside = ((lat_global >= 0) & (lat_global < lat_total))[None, :]
    cor = extend_lat(coriolis[None, :], HALO)

    fields = extend(jnp.concatenate([increment, depth_field[None]], axis=0), HALO)
    east_wind, north_wind, height, depth = fields[0], fields[1], fields[2], fields[3]
    inner = (slice(HALO, HALO + rows), slice(HALO, HALO + cols))

    def tangent_run(_, state):
        return tangent_step(*state, depth, cor, inside)

    def adjoint_run(_, state):
        return adjoint_step(*state, depth, cor, inside)

    state = (east_wind, north_wind, height)
    forcings = []
    for obs_index in range(OBS_TIMES):
        state = lax.fori_loop(0, interval, tangent_run, state)
        stacked = jnp.stack([field[inner] for field in state])
        forcing = observe(
            stacked,
            tracks[obs_index],
            innov[obs_index],
            weights[obs_index],
            footprint,
            channel_weights,
        )
        forcings.append(extend(forcing, HALO))

    state = (jnp.zeros_like(depth),) * 3
    for obs_index in range(OBS_TIMES - 1, -1, -1):
        state = tuple(field + forced for field, forced in zip(state, forcings[obs_index]))
        state = lax.fori_loop(0, interval, adjoint_run, state)
    east_adj, north_adj, height_adj = state
    adjoint = jnp.stack([east_adj[inner], north_adj[inner], height_adj[inner]])
    return increment + adjoint


def solution(mesh):
    return jax.shard_map(
        on_device,
        mesh=mesh,
        in_specs=(
            P(None, "lon", "lat"),
            P("lon", "lat"),
            P("lat"),
            P(),
            P(),
            P(None, "lat", "lon", None),
            P(None, "lat", "lon", None, None, None, None),
            P(None, "lat", "lon", None),
        ),
        out_specs=P(None, "lon", "lat"),
        check_vma=False,
    )
```
